32 devices in a mesh: groups: 2 (over y), tm: 4 (over z), head: 2 (over x), series: 2 (over core).
Axes of the slice: x: 2, y: 2, z: 4, core: 2. Of those that a mesh axis runs over, the one named last changes fastest.
Arguments:
- queries: bfloat16 [4, 4096, 1024], P(('groups', 'series'), 'tm', 'head'), parts along dimension 0, may hold values from -16 to 16
- key_vecs: bfloat16 [4, 4096, 1024], P(('groups', 'series'), 'tm', 'head'), parts along dimension 0, may hold values from -4 to 4
- value_vecs: bfloat16 [4, 4096, 1024], P(('groups', 'series'), 'tm', 'head'), parts along dimension 0, may hold values from -6 to 6
- out_grad: bfloat16 [4, 4096, 1024], P(('groups', 'series'), 'tm', 'head'), parts along dimension 0, may hold values from -6 to 6
- block_links: int32 [64, 4], P('tm'), may hold values from 0 to 63, as said below
- coarse_taps: float32 [2, 4, 4, 1024], P(None, None, None, 'head'), may hold values from 0.2 to 0.8
Outputs:
- attended: bfloat16 [4, 4096, 1024], P(('groups', 'series'), 'tm', 'head'), parts along dimension 0
- grad_query: bfloat16 [4, 4096, 1024], P(('groups', 'series'), 'tm', 'head'), parts along dimension 0
- grad_key: bfloat16 [4, 4096, 1024], P(('groups', 'series'), 'tm', 'head'), parts along dimension 0
- grad_value: bfloat16 [4, 4096, 1024], P(('groups', 'series'), 'tm', 'head'), parts along dimension 0
The draws below stay inside these ranges and needn't reach their ends.
There are 2 independent parts, one for each index of `groups`. The reference program is written for one: setup_inputs(seed, part) draws one part's arguments, and reference() takes and returns one part's arrays. A program takes and returns all parts, laid end to end along the dimension named above; an argument that names none is the same for every part. Nothing has to cross between parts.
Inputs may be any that keep to these rules, and one draw needn't show every extreme that they name: block_links[b, 0] lies in b - 2 .. b and block_links[b, 1] in b .. b + 2 (level-0 block ids); block_links[b, 2] is a level-1 block id within 2 of b // 4, block_links[b, 3] a level-2 block id within 2 of b // 16.
All inputs are finite; a program needn't handle non-finite values.
Results may differ from the reference program's by a relative error of at most 0.0095.
Values may be sent and summed in bfloat16 or wider, within the bound.
No kernel may reach another device: no remote copies, remote signals or barrier semaphores. Data moves between devices by JAX's collectives and lax.ppermute only.
A program may use at most 192 MiB of HBM per device.

```python
import math
import jax
import jax.numpy as jnp
from jax import lax

HEADS = 16
HEAD_DIM = 64
HF = 1024
BLOCK = 64
SERIES = 2
LEN = 4096
NB0 = 64


def draw_key_vecs(key, part):
    result = jnp.clip(jax.random.normal(jax.random.fold_in(key, 1), (SERIES, LEN, HF), jnp.float32), -4.0, 4.0)
    return result.astype(jnp.bfloat16)


def draw_queries(key, part):
    result = jnp.clip(jax.random.normal(jax.random.fold_in(key, 2), (SERIES, LEN, HF), jnp.float32), -4.0, 4.0)
    return result.astype(jnp.bfloat16)


def draw_block_links(key, part):
    block_index = jnp.arange(NB0, dtype=jnp.int32)
    step_left = jax.random.randint(jax.random.fold_in(key, 21), (NB0,), 1, 3, dtype=jnp.int32)
    step_right = jax.random.randint(jax.random.fold_in(key, 22), (NB0,), 1, 3, dtype=jnp.int32)
    left_link = jnp.maximum(block_index - step_left, 0)
    right_link = jnp.minimum(block_index + step_right, NB0 - 1)
    pick_one = jax.random.randint(jax.random.fold_in(key, 23), (NB0,), 0, 4, dtype=jnp.int32)
    shift_one = jnp.where(pick_one < 2, pick_one - 2, pick_one - 1)
    link_one = jnp.clip(block_index // 4 + shift_one, 0, NB0 // 4 - 1)
    pick_two = jax.random.randint(jax.random.fold_in(key, 24), (NB0,), 0, 4, dtype=jnp.int32)
    shift_two = jnp.where(pick_two < 2, pick_two - 2, pick_two - 1)
    link_two = jnp.clip(block_index // 16 + shift_two, 0, NB0 // 16 - 1)
    return jnp.stack([left_link, right_link, link_one, link_two], axis=1).astype(jnp.int32)


def level_of(key, shape, pieces, least, largest):
    loudness, own = 1.0, jax.random.fold_in(key, 6)
    for axis_at, parts in pieces:
        draws = jnp.exp(jax.random.uniform(jax.random.fold_in(own, axis_at), (parts,), jnp.float32, least / len(pieces), largest / len(pieces)))
        loudness = loudness * jnp.repeat(draws, shape[axis_at] // parts).reshape([-1 if axis == axis_at else 1 for axis in range(len(shape))])
    return loudness


def centred(key, shape, scale, limit, split=(), kind=jnp.bfloat16):
    values = jax.random.normal(key, shape, jnp.float32) * scale
    if len(split) > 0:
        values = level_of(key, shape, split, -0.22, 0.18) * values
    return jnp.clip(values, min=-limit, max=limit).astype(kind)


def setup_inputs(seed: int = 0, part: int = 0) -> dict:
    splits = jax.random.split(jax.random.key(seed), 7)
    own_keys = jax.random.split(jax.random.fold_in(splits[6], part), 7)
    queries = draw_queries(jax.random.fold_in(jax.random.fold_in(splits[6], part), 71), part)
    key_vecs = draw_key_vecs(jax.random.fold_in(jax.random.fold_in(splits[6], part), 71), part)
    value_vecs = centred(own_keys[2], (SERIES, LEN, HF), 1.0, 6.0, ((0, 2), (1, 4), (2, 2)))
    out_grad = centred(own_keys[3], (SERIES, LEN, HF), 1.0, 6.0, ((0, 2), (1, 4), (2, 2)))
    block_links = draw_block_links(jax.random.fold_in(splits[6], 71), part)
    coarse_taps = jnp.clip(0.2 + 0.6 * jax.random.uniform(splits[5], (2, 4, 4, HF), jnp.float32) ** level_of(splits[5], (2, 4, 4, HF), ((3, 2),), -0.2, 0.2), 0.2, 0.8)
    return dict(queries=queries, key_vecs=key_vecs, value_vecs=value_vecs, out_grad=out_grad, block_links=block_links, coarse_taps=coarse_taps)


def coarsen_step(fine_rows, tap_row):
    row_count = fine_rows.shape[0] // 4
    grouped = fine_rows.reshape(row_count, 4, fine_rows.shape[1]).astype(jnp.float32)
    return lax.optimization_barrier(jnp.sum(grouped * tap_row[None], axis=1)).astype(jnp.bfloat16)

def spread_back(coarse_grad, tap_row):
    row_count = coarse_grad.shape[0]
    return (coarse_grad[:, None, :] * tap_row[None]).reshape(row_count * 4, coarse_grad.shape[1])

def attend_block(q_block, keyvals, grad_block):
    score_scale = 1.0 / math.sqrt(HEAD_DIM)
    queries_h = q_block.reshape(-1, HEADS, HEAD_DIM).astype(jnp.float32)
    keys_h = keyvals[:, :HF].reshape(-1, HEADS, HEAD_DIM).astype(jnp.float32)
    values_h = keyvals[:, HF:].reshape(-1, HEADS, HEAD_DIM).astype(jnp.float32)
    grads_h = grad_block.reshape(-1, HEADS, HEAD_DIM).astype(jnp.float32)
    scores = jnp.einsum('qhd,khd->hqk', queries_h, keys_h) * score_scale
    row_max = lax.optimization_barrier(jnp.max(scores, axis=-1, keepdims=True))
    exponent = jnp.exp(scores - row_max)
    probs_f32 = exponent / lax.optimization_barrier(jnp.sum(exponent, axis=-1, keepdims=True))
    probs_b = lax.optimization_barrier(probs_f32.astype(jnp.bfloat16)).astype(jnp.float32)
    attended = jnp.einsum('hqk,khd->qhd', probs_b, values_h).reshape(-1, HF).astype(jnp.bfloat16)
    dprob = jnp.einsum('qhd,khd->hqk', grads_h, values_h)
    row_delta = lax.optimization_barrier(jnp.sum(probs_f32 * dprob, axis=-1, keepdims=True))
    dscore = lax.optimization_barrier((score_scale * probs_f32 * (dprob - row_delta)).astype(jnp.bfloat16)).astype(jnp.float32)
    grad_q = jnp.einsum('hqk,khd->qhd', dscore, keys_h).reshape(-1, HF).astype(jnp.bfloat16)
    grad_k = jnp.einsum('hqk,qhd->khd', dscore, queries_h).reshape(-1, HF)
    grad_v = jnp.einsum('hqk,qhd->khd', probs_b, grads_h).reshape(-1, HF)
    return (attended, grad_q, jnp.concatenate([grad_k, grad_v], axis=-1))

def one_series(queries, key_vecs, value_vecs, out_grad, block_links, tap_table):
    level_zero = jnp.concatenate([key_vecs, value_vecs], axis=-1)
    kv_width = level_zero.shape[1]
    levels_list = [level_zero]
    for section_idx in range(4):
        levels_list.append(coarsen_step(levels_list[-1], tap_table[section_idx]))
    blocks_zero = levels_list[0].reshape(-1, BLOCK, kv_width)
    blocks_one = levels_list[1].reshape(-1, BLOCK, kv_width)
    blocks_two = levels_list[2].reshape(-1, BLOCK, kv_width)
    upper_rows = jnp.concatenate([levels_list[3], levels_list[4]], axis=0)
    q_blocks = queries.reshape(-1, BLOCK, HF)
    g_blocks = out_grad.reshape(-1, BLOCK, HF)

    def block_step(totals, inputs):
        grad_zero, grad_one, grad_two, grad_up = totals
        q_block, g_block, link_row, block_index = inputs
        zero_ids = jnp.stack([block_index, link_row[0], link_row[1]])
        one_ids = jnp.stack([block_index // 4, link_row[2]])
        two_ids = jnp.stack([block_index // 16, link_row[3]])
        keyvals = jnp.concatenate([blocks_zero[zero_ids].reshape(-1, kv_width), blocks_one[one_ids].reshape(-1, kv_width), blocks_two[two_ids].reshape(-1, kv_width), upper_rows], axis=0)
        attended, grad_q, grad_kv = attend_block(q_block, keyvals, g_block)
        grad_zero = grad_zero.at[zero_ids].add(grad_kv[:3 * BLOCK].reshape(3, BLOCK, kv_width))
        grad_one = grad_one.at[one_ids].add(grad_kv[3 * BLOCK:5 * BLOCK].reshape(2, BLOCK, kv_width))
        grad_two = grad_two.at[two_ids].add(grad_kv[5 * BLOCK:7 * BLOCK].reshape(2, BLOCK, kv_width))
        grad_up = grad_up + grad_kv[7 * BLOCK:]
        return ((grad_zero, grad_one, grad_two, grad_up), (attended, grad_q))
    init_totals = (jnp.zeros(blocks_zero.shape, jnp.float32), jnp.zeros(blocks_one.shape, jnp.float32), jnp.zeros(blocks_two.shape, jnp.float32), jnp.zeros(upper_rows.shape, jnp.float32))
    block_ids = jnp.arange(NB0, dtype=jnp.int32)
    totals, outputs = lax.scan(block_step, init_totals, (q_blocks, g_blocks, block_links, block_ids))
    grad_zero, grad_one, grad_two, grad_up = totals
    three_rows = LEN // 64
    grad_three = grad_up[:three_rows]
    grad_four = grad_up[three_rows:]
    grad_three = grad_three + spread_back(grad_four, tap_table[3])
    grad_two = grad_two.reshape(-1, kv_width) + spread_back(grad_three, tap_table[2])
    grad_one = grad_one.reshape(-1, kv_width) + spread_back(grad_two, tap_table[1])
    grad_zero = grad_zero.reshape(-1, kv_width) + spread_back(grad_one, tap_table[0])
    attended = outputs[0].reshape(LEN, HF)
    grad_query = outputs[1].reshape(LEN, HF)
    return (attended, grad_query, grad_zero[:, :HF].astype(jnp.bfloat16), grad_zero[:, HF:].astype(jnp.bfloat16))

def reference(queries, key_vecs, value_vecs, out_grad, block_links, coarse_taps):
    tap_table = jnp.concatenate([coarse_taps[0], coarse_taps[1]], axis=-1)

    def per_series(operands):
        return one_series(operands[0], operands[1], operands[2], operands[3], block_links, tap_table)
    attended, grad_query, grad_key, grad_value = lax.map(per_series, (queries, key_vecs, value_vecs, out_grad))
    return (attended, grad_query, grad_key, grad_value)
```

```python
import math

import jax
import jax.numpy as jnp
from jax import lax
from jax.experimental import pallas as pl
from jax.experimental.pallas import tpu as pltpu
from jax.sharding import PartitionSpec as P

HEAD_DIM = 64
BLOCK = 64


def padded_2(block, sides, width):
    for axis, dim in sides:
        count = lax.axis_size(axis)
        forward = [(i, i + 1) for i in range(count - 1)]
        backward = [(target, source) for source, target in forward]
        low = lax.ppermute(
            lax.slice_in_dim(block, block.shape[dim] - width, None, axis=dim), axis, forward
        )
        high = lax.ppermute(lax.slice_in_dim(block, 0, width, axis=dim), axis, backward)
        block = jnp.concatenate([low, block, high], axis=dim)
    return block


def coarsen_step(fine_rows, tap_row):
    fine_shape = fine_rows.shape
    grouped = fine_rows.reshape(fine_shape[0], fine_shape[1] // 4, 4, fine_shape[2]).astype(
        jnp.float32
    )
    return jnp.sum(grouped * tap_row[None, None], axis=2).astype(jnp.bfloat16)


def spread_back(coarse_grad, tap_row):
    grad_shape = coarse_grad.shape
    return (coarse_grad[:, :, None, :] * tap_row[None, None]).reshape(
        grad_shape[0], grad_shape[1] * 4, grad_shape[2]
    )


NT_DIMS = (((1,), (1,)), ((), ()))


def attend_kernel(ids_ref, q_ref, g_ref, k0_ref, v0_ref, k1_ref, v1_ref, k2_ref, v2_ref,
                  ku_ref, vu_ref, att_ref, gq_ref, dk0_ref, dv0_ref, dk1_ref, dv1_ref,
                  dk2_ref, dv2_ref, dku_ref, dvu_ref):
    block = pl.program_id(1)
    acc_refs = (dk0_ref, dv0_ref, dk1_ref, dv1_ref, dk2_ref, dv2_ref, dku_ref, dvu_ref)

    @pl.when(block == 0)
    def _():
        for acc in acc_refs:
            acc[...] = jnp.zeros(acc.shape, acc.dtype)

    base = block * 7
    picks = [ids_ref[base + i] for i in range(7)]
    sources = ((k0_ref, v0_ref), (k0_ref, v0_ref), (k0_ref, v0_ref), (k1_ref, v1_ref),
               (k1_ref, v1_ref), (k2_ref, v2_ref), (k2_ref, v2_ref))
    keys = jnp.concatenate([kr[i] for (kr, _), i in zip(sources, picks)] + [ku_ref[...]], axis=0)
    vals = jnp.concatenate([vr[i] for (_, vr), i in zip(sources, picks)] + [vu_ref[...]], axis=0)
    q = q_ref[0]
    g = g_ref[0]
    lanes = q.shape[1]
    lane = lax.broadcasted_iota(jnp.int32, (1, lanes), 1)
    first = lane < HEAD_DIM
    zero = jnp.zeros_like(q)
    q2 = jnp.concatenate([jnp.where(first, q, zero), jnp.where(first, zero, q)], axis=0)
    g2 = jnp.concatenate([jnp.where(first, g, zero), jnp.where(first, zero, g)], axis=0)
    rows = q.shape[0]
    scale = 1.0 / math.sqrt(HEAD_DIM)

    scores = lax.dot_general(q2, keys, NT_DIMS, preferred_element_type=jnp.float32) * scale
    exponent = jnp.exp(scores - jnp.max(scores, axis=1, keepdims=True))
    probs = exponent / jnp.sum(exponent, axis=1, keepdims=True)
    attended = jnp.dot(probs.astype(jnp.bfloat16), vals, preferred_element_type=jnp.float32)
    dprob = lax.dot_general(g2, vals, NT_DIMS, preferred_element_type=jnp.float32)
    delta = jnp.sum(probs * dprob, axis=1, keepdims=True)
    dscore = (scale * probs * (dprob - delta)).astype(jnp.bfloat16)
    grad_q = jnp.dot(dscore, keys, preferred_element_type=jnp.float32)
    att_ref[0] = jnp.where(first, attended[:rows], attended[rows:]).astype(att_ref.dtype)
    gq_ref[0] = jnp.where(first, grad_q[:rows], grad_q[rows:]).astype(gq_ref.dtype)

    scores_t = lax.dot_general(keys, q2, NT_DIMS, preferred_element_type=jnp.float32) * scale
    exponent_t = jnp.exp(scores_t - jnp.max(scores_t, axis=0, keepdims=True))
    probs_t = exponent_t / jnp.sum(exponent_t, axis=0, keepdims=True)
    dprob_t = lax.dot_general(vals, g2, NT_DIMS, preferred_element_type=jnp.float32)
    delta_t = jnp.sum(probs_t * dprob_t, axis=0, keepdims=True)
    dscore_t = (scale * probs_t * (dprob_t - delta_t)).astype(jnp.bfloat16)
    grad_k = jnp.dot(dscore_t, q2, preferred_element_type=jnp.float32)
    grad_v = jnp.dot(probs_t.astype(jnp.bfloat16), g2, preferred_element_type=jnp.float32)

    targets = ((dk0_ref, dv0_ref), (dk0_ref, dv0_ref), (dk0_ref, dv0_ref), (dk1_ref, dv1_ref),
               (dk1_ref, dv1_ref), (dk2_ref, dv2_ref), (dk2_ref, dv2_ref))
    for piece, ((dkr, dvr), i) in enumerate(zip(targets, picks)):
        low = piece * BLOCK
        dkr[i] = dkr[i] + grad_k[low : low + BLOCK]
        dvr[i] = dvr[i] + grad_v[low : low + BLOCK]
    near = 7 * BLOCK
    dku_ref[...] = dku_ref[...] + grad_k[near:]
    dvu_ref[...] = dvu_ref[...] + grad_v[near:]


def attend_all(ids, q_blocks, g_blocks, pool_zero, pool_one, pool_two, upper_rows):
    n_blocks, _, features = q_blocks.shape
    pairs = features // 128
    lanes = 128

    def pool_specs(pool):
        count = pool.shape[0]
        return [
            pl.BlockSpec((count, BLOCK, lanes), lambda p, b, ids: (0, 0, p)),
            pl.BlockSpec((count, BLOCK, lanes), lambda p, b, ids: (0, 0, pairs + p)),
        ]

    upper_count = upper_rows.shape[0]
    in_specs = (
        [pl.BlockSpec((1, BLOCK, lanes), lambda p, b, ids: (b, 0, p))] * 2
        + pool_specs(pool_zero)
        + pool_specs(pool_one)
        + pool_specs(pool_two)
        + [
            pl.BlockSpec((upper_count, lanes), lambda p, b, ids: (0, p)),
            pl.BlockSpec((upper_count, lanes), lambda p, b, ids: (0, pairs + p)),
        ]
    )

    def acc_spec(count):
        return pl.BlockSpec((count, BLOCK, lanes), lambda p, b, ids: (0, 0, p))

    out_specs = [pl.BlockSpec((1, BLOCK, lanes), lambda p, b, ids: (b, 0, p))] * 2
    out_shape = [jax.ShapeDtypeStruct(q_blocks.shape, jnp.bfloat16)] * 2
    for pool in (pool_zero, pool_one, pool_two):
        out_specs += [acc_spec(pool.shape[0])] * 2
        out_shape += [jax.ShapeDtypeStruct((pool.shape[0], BLOCK, features), jnp.float32)] * 2
    out_specs += [pl.BlockSpec((upper_count, lanes), lambda p, b, ids: (0, p))] * 2
    out_shape += [jax.ShapeDtypeStruct((upper_count, features), jnp.float32)] * 2
    grid_spec = pltpu.PrefetchScalarGridSpec(
        num_scalar_prefetch=1,
        grid=(pairs, n_blocks),
        in_specs=in_specs,
        out_specs=out_specs,
    )
    return pl.pallas_call(
        attend_kernel,
        grid_spec=grid_spec,
        out_shape=out_shape,
    )(ids, q_blocks, g_blocks, pool_zero, pool_zero, pool_one, pool_one, pool_two, pool_two,
      upper_rows, upper_rows)


def shards(queries, key_vecs, value_vecs, out_grad, block_links, coarse_taps):
    series_count, tok_local, features = queries.shape
    kv_width = 2 * features
    rim_rows = 2 * BLOCK
    tm_count = lax.axis_size("tm")
    position = lax.axis_index("tm")
    tap_table = jnp.concatenate([coarse_taps[0], coarse_taps[1]], axis=-1)
    level_zero = jnp.concatenate([key_vecs, value_vecs], axis=-1)
    level_one = coarsen_step(level_zero, tap_table[0])
    level_two = coarsen_step(level_one, tap_table[1])
    rows_two = level_two.shape[1]
    rows_three = rows_two // 4
    rows_four = rows_three // 4
    level_three = coarsen_step(level_two, tap_table[2])
    level_four = coarsen_step(level_three, tap_table[3])
    packed = jnp.concatenate([level_two, level_three, level_four], axis=1)[:, None]
    gathered = lax.all_gather(packed, "tm", axis=1, tiled=True)
    every_two = gathered[:, :, :rows_two].reshape(series_count, -1, kv_width)
    every_three = gathered[:, :, rows_two : rows_two + rows_three].reshape(
        series_count, -1, kv_width
    )
    every_four = gathered[:, :, rows_two + rows_three :].reshape(series_count, -1, kv_width)
    upper_rows = jnp.concatenate([every_three, every_four], axis=1)
    rims_out = jnp.concatenate(
        [
            level_zero[:, :rim_rows],
            level_one[:, :rim_rows],
            level_zero[:, -rim_rows:],
            level_one[:, -rim_rows:],
        ],
        axis=1,
    )
    padded = padded_2(rims_out, (("tm", 1),), 2 * rim_rows)
    pool_zero = jnp.concatenate(
        [padded[:, :rim_rows], level_zero, padded[:, -2 * rim_rows : -rim_rows]], axis=1
    ).reshape(series_count, -1, BLOCK, kv_width)
    pool_one = jnp.concatenate(
        [padded[:, rim_rows : 2 * rim_rows], level_one, padded[:, -rim_rows:]], axis=1
    ).reshape(series_count, -1, BLOCK, kv_width)
    pool_two = every_two.reshape(series_count, -1, BLOCK, kv_width)
    blocks_local = tok_local // BLOCK
    first_zero = position * blocks_local - 2
    first_one = position * (blocks_local // 4) - 2
    own_index = position * blocks_local + jnp.arange(blocks_local, dtype=jnp.int32)
    ids_zero = jnp.stack([own_index, block_links[:, 0], block_links[:, 1]], axis=1) - first_zero
    ids_one = jnp.stack([own_index // 4, block_links[:, 2]], axis=1) - first_one
    ids_two = jnp.stack([own_index // 16, block_links[:, 3]], axis=1)
    ids_all = jnp.concatenate([ids_zero, ids_one, ids_two], axis=1).reshape(-1)
    q_blocks = queries.reshape(series_count, blocks_local, BLOCK, features)
    g_blocks = out_grad.reshape(series_count, blocks_local, BLOCK, features)
    attended_parts = []
    grad_q_parts = []
    level_grads = [[] for _ in range(4)]
    for which in range(series_count):
        results = attend_all(
            ids_all,
            q_blocks[which],
            g_blocks[which],
            pool_zero[which],
            pool_one[which],
            pool_two[which],
            upper_rows[which],
        )
        attended_parts.append(results[0].reshape(tok_local, features))
        grad_q_parts.append(results[1].reshape(tok_local, features))
        for level in range(4):
            level_grads[level].append(
                jnp.concatenate([results[2 + 2 * level], results[3 + 2 * level]], axis=-1)
            )
    grad_zero, grad_one, grad_two, grad_up = [jnp.stack(parts) for parts in level_grads]
    attended = jnp.stack(attended_parts)
    grad_query = jnp.stack(grad_q_parts)
    flat_zero = grad_zero.reshape(series_count, -1, kv_width)
    flat_one = grad_one.reshape(series_count, -1, kv_width)
    rims_back = jnp.concatenate(
        [
            flat_zero[:, :rim_rows],
            flat_one[:, :rim_rows],
            flat_zero[:, -rim_rows:],
            flat_one[:, -rim_rows:],
        ],
        axis=1,
    )
    returned = padded_2(rims_back.astype(jnp.bfloat16), (("tm", 1),), 2 * rim_rows).astype(
        rims_back.dtype
    )
    own_zero = flat_zero[:, rim_rows:-rim_rows]
    own_zero = own_zero.at[:, :rim_rows].add(returned[:, :rim_rows])
    own_zero = own_zero.at[:, -rim_rows:].add(returned[:, -2 * rim_rows : -rim_rows])
    own_one = flat_one[:, rim_rows:-rim_rows]
    own_one = own_one.at[:, :rim_rows].add(returned[:, rim_rows : 2 * rim_rows])
    own_one = own_one.at[:, -rim_rows:].add(returned[:, -rim_rows:])
    every_grad_two = grad_two.reshape(series_count, -1, kv_width)
    grad_three_all = grad_up[:, : tm_count * rows_three]
    grad_four_all = grad_up[:, tm_count * rows_three :]
    packed_grad = jnp.concatenate(
        [
            every_grad_two.reshape(series_count, tm_count, rows_two, kv_width),
            grad_three_all.reshape(series_count, tm_count, rows_three, kv_width),
            grad_four_all.reshape(series_count, tm_count, rows_four, kv_width),
        ],
        axis=2,
    )
    mine_all = lax.psum_scatter(
        packed_grad.astype(jnp.bfloat16), "tm", scatter_dimension=1, tiled=True
    ).astype(jnp.float32)[:, 0]
    mine_two = mine_all[:, :rows_two]
    mine_three = mine_all[:, rows_two : rows_two + rows_three]
    mine_four = mine_all[:, rows_two + rows_three :]
    mine_three = mine_three + spread_back(mine_four, tap_table[3])
    mine_two = mine_two + spread_back(mine_three, tap_table[2])
    own_one = own_one + spread_back(mine_two, tap_table[1])
    own_zero = own_zero + spread_back(own_one, tap_table[0])
    grad_key = own_zero[..., :features].astype(jnp.bfloat16)
    grad_value = own_zero[..., features:].astype(jnp.bfloat16)
    return (attended, grad_query, grad_key, grad_value)


def solution(mesh):
    in_specs = (
        P(("groups", "series"), "tm", "head"),
        P(("groups", "series"), "tm", "head"),
        P(("groups", "series"), "tm", "head"),
        P(("groups", "series"), "tm", "head"),
        P("tm", None),
        P(None, None, None, "head"),
    )
    out_specs = (
        P(("groups", "series"), "tm", "head"),
        P(("groups", "series"), "tm", "head"),
        P(("groups", "series"), "tm", "head"),
        P(("groups", "series"), "tm", "head"),
    )
    return jax.shard_map(shards, mesh=mesh, in_specs=in_specs, out_specs=out_specs, check_vma=False)
```
